256 devices in a mesh: seq: 64 (over z, y, core), mp: 4 (over x).
Axes of the slice: x: 4, y: 4, z: 8, core: 2. Of those that a mesh axis runs over, the one named last changes fastest.
Arguments:
- patches: bfloat16 [262144, 1280], P('seq'), may hold values from -2 to 2
- w_qkv: bfloat16 [1280, 3840], P('seq', 'mp'), as said below
- w_out: bfloat16 [1280, 1280], P('mp', 'seq'), may hold values from -0.15625 to 0.15625
- page_rows: int32 [64], replicated, may hold values from 32 to 64, as said below
- page_cols: int32 [64], replicated, may hold values from 32 to 64, as said below
- window_slot: int32 [64, 64], replicated, may hold values from 0 to 63, each once within a row
Outputs:
- blocks: bfloat16 [262144, 1280], P('seq', 'mp')
The draws below stay inside these ranges and needn't reach their ends.
Inputs may be any that keep to these rules, and one draw needn't show every extreme that they name: `page_rows`: page heights, multiples of 16; some page has the largest. `page_cols`: page widths, multiples of 16; some page has the largest. `window_slot`: each row is a permutation. `w_qkv`: entries of order at most 5.5 / sqrt(1280).
All inputs are finite; a program needn't handle non-finite values.
Results may differ from the reference program's by a relative error of at most 0.012.
Values may be sent and summed in bfloat16 or wider, within the bound.
No kernel may reach another device: no remote copies, remote signals or barrier semaphores. Data moves between devices by JAX's collectives and lax.ppermute only.
A program may use at most 192 MiB of HBM per device.

```python
import math
import jax
import jax.numpy as jnp
from jax import lax

D = 1280
HEADS = 16
HD = 80
WS = 8
GRID = 8
WIN_CAP = 64
TOK_CAP = 4096
PAGES = 64
PER = 1
N_SEQ = 64
N_MP = 4


def page_shape(key):
    lowest = GRID // 4
    highest = GRID // 2 + 1
    row_steps = jax.random.randint(jax.random.fold_in(key, 101), (PAGES,), lowest, highest)
    column_steps = jax.random.randint(jax.random.fold_in(key, 102), (PAGES,), lowest, highest)
    chosen = jax.random.randint(jax.random.fold_in(key, 103), (), 0, PAGES)
    chosen_page = jnp.arange(PAGES) == chosen
    row_steps = jnp.where(chosen_page, GRID // 2, row_steps)
    column_steps = jnp.where(chosen_page, GRID // 2, column_steps)
    return ((row_steps * (2 * WS)).astype(jnp.int32), (column_steps * (2 * WS)).astype(jnp.int32))


def draw_page_rows(key, part):
    return page_shape(key)[0]


def draw_page_cols(key, part):
    return page_shape(key)[1]


def draw_w_qkv(key, part):
    normal_base = jax.random.normal(jax.random.fold_in(key, 201), (D, HEADS, 3, HD), jnp.float32) / math.sqrt(D)
    return normal_base.reshape(D, 3 * D).astype(jnp.bfloat16)


def block_levels(key, extent, split, smallest, top_value):
    loudness = 1.0
    for dim, parts in split:
        draws = jax.random.uniform(jax.random.fold_in(jax.random.fold_in(key, 6), dim), (parts,), jnp.float32, smallest / len(split), top_value / len(split))
        loudness = loudness * jnp.repeat(jnp.exp(draws), extent[dim] // parts).reshape((-1,) + (1,) * (len(extent) - 1 - dim))
    return loudness


def scatter_about(stream_key, shape, width, most, shards=(), held_as=jnp.bfloat16):
    gain = block_levels(stream_key, shape, shards, -0.22, 0.18) if shards else 1.0
    values = jax.random.normal(stream_key, shape, jnp.float32) * width * gain
    return jnp.minimum(jnp.maximum(values, -most), most).astype(held_as)


def setup_inputs(seed: int = 0) -> dict:
    key_list = jax.random.split(jax.random.key(seed), 7)
    patches = scatter_about(key_list[0], (PAGES * TOK_CAP, D), 0.3, 2.0, ((0, 64),))
    w_qkv = draw_w_qkv(jax.random.fold_in(key_list[6], 71), 0)
    w_out = scatter_about(key_list[2], (D, D), D ** -0.5, 0.15625, ((0, 4), (1, 64)))
    page_rows = draw_page_rows(jax.random.fold_in(key_list[6], 71), 0)
    page_cols = draw_page_cols(jax.random.fold_in(key_list[6], 71), 0)
    window_slot = jax.vmap(lambda own: jax.random.permutation(own, WIN_CAP))(jax.random.split(key_list[5], PAGES)).reshape((PAGES, WIN_CAP)).astype(jnp.int32)
    return dict(patches=patches, w_qkv=w_qkv, w_out=w_out, page_rows=page_rows, page_cols=page_cols, window_slot=window_slot)


EPSILON = 1e-06

def rotate(vector, cosine_table, sine_table):
    half_size = vector.shape[-1] // 2
    turned = jnp.concatenate([-vector[..., half_size:], vector[..., :half_size]], axis=-1)
    return vector * cosine_table + turned * sine_table

def angle_tables(row_place, column_place, head_size):
    quarter = head_size // 4
    frequency = 1.0 / 10000.0 ** (jnp.arange(quarter, dtype=jnp.float32) * 2.0 / (head_size // 2))
    angles = jnp.concatenate([row_place[..., None].astype(jnp.float32) * frequency, column_place[..., None].astype(jnp.float32) * frequency], axis=-1)
    angles = jnp.concatenate([angles, angles], axis=-1)
    return (jnp.cos(angles), jnp.sin(angles))

def slot_positions(page_widths, slot_table, slot_numbers, window_side):
    matches = slot_table[:, :, None] == slot_numbers[None, None, :]
    ordinal = jnp.arange(slot_table.shape[1], dtype=jnp.int32)
    window = lax.optimization_barrier(jnp.sum(jnp.where(matches, ordinal[None, :, None], 0), axis=1)).astype(jnp.int32)
    across = (page_widths // window_side).astype(jnp.int32)
    window_row = window // across[:, None]
    window_column = window % across[:, None]
    unit_side = window_side // 2
    position = jnp.arange(window_side * window_side, dtype=jnp.int32)
    merge_unit = position // 4
    corner = position % 4
    inner_row = merge_unit // unit_side * 2 + corner // 2
    inner_column = merge_unit % unit_side * 2 + corner % 2
    row_place = window_row[:, :, None] * window_side + inner_row
    column_place = window_column[:, :, None] * window_side + inner_column
    return (row_place, column_place)

def merge_source(height, page_width, slot_row, window_side, position_count):
    position = jnp.arange(position_count, dtype=jnp.int32)
    merge_unit = position // 4
    corner = position % 4
    units_wide = page_width // 2
    unit_row = merge_unit // units_wide
    unit_column = merge_unit % units_wide
    unit_side = window_side // 2
    across = page_width // window_side
    live_rows = unit_row < height // 2
    window = unit_row // unit_side * across + unit_column // unit_side
    window = jnp.where(live_rows, window, 0)
    ordinal = jnp.arange(slot_row.shape[0], dtype=jnp.int32)
    slot_index = lax.optimization_barrier(jnp.sum(jnp.where(window[:, None] == ordinal[None, :], slot_row[None, :], 0), axis=1)).astype(jnp.int32)
    inner = (unit_row % unit_side * unit_side + unit_column % unit_side) * 4 + corner
    inner = jnp.where(live_rows, inner, 0)
    return ((slot_index * (window_side * window_side) + inner).astype(jnp.int32), live_rows)

def normalize(block_in):
    values = block_in.astype(jnp.float32)
    factor = lax.rsqrt(lax.optimization_barrier(jnp.mean(values * values, axis=-1, keepdims=True)) + EPSILON)
    return (values * factor).astype(jnp.bfloat16)

def settle(array_in):
    return lax.optimization_barrier(array_in.astype(jnp.bfloat16)).astype(jnp.float32)

def attend(projected, cosine_table, sine_table, window_tokens, head_size):
    windows = projected.shape[0] // window_tokens
    head_count = projected.shape[1] // (3 * head_size)
    split_qkv = projected.reshape(windows, window_tokens, head_count, 3, head_size)
    queries = settle(rotate(split_qkv[:, :, :, 0], cosine_table, sine_table))
    key_block = settle(rotate(split_qkv[:, :, :, 1], cosine_table, sine_table))
    values = settle(split_qkv[:, :, :, 2])
    scores = jnp.einsum('wqhd,wkhd->whqk', queries, key_block, precision=lax.Precision.HIGHEST) / math.sqrt(head_size)
    row_max = lax.optimization_barrier(jnp.max(scores, axis=-1, keepdims=True))
    lifted = jnp.exp(scores - row_max)
    weights = settle(lifted / lax.optimization_barrier(jnp.sum(lifted, axis=-1, keepdims=True)))
    mixed_heads = jnp.einsum('whqk,wkhd->wqhd', weights, values, precision=lax.Precision.HIGHEST)
    return mixed_heads.astype(jnp.bfloat16).reshape(windows * window_tokens, head_count * head_size)

def reference(patches, w_qkv, w_out, page_rows, page_cols, window_slot):
    window_tokens = WS * WS
    spread = patches.reshape(N_SEQ, PAGES, PER, window_tokens, D)
    slot_numbers = jnp.arange(WIN_CAP, dtype=jnp.int32)
    groups = D // N_MP

    def one_page(page_index):
        tokens = lax.dynamic_index_in_dim(spread, page_index, 1, keepdims=False).reshape(WIN_CAP * window_tokens, D)
        slot_table = lax.dynamic_slice_in_dim(window_slot, page_index, 1, 0)
        widths = lax.dynamic_slice_in_dim(page_cols, page_index, 1, 0)
        heights = lax.dynamic_slice_in_dim(page_rows, page_index, 1, 0)
        row_place, column_place = slot_positions(widths, slot_table, slot_numbers, WS)
        cosine_table, sine_table = angle_tables(row_place.reshape(WIN_CAP, window_tokens), column_place.reshape(WIN_CAP, window_tokens), HD)
        normed = normalize(tokens)
        projected = jnp.dot(normed, w_qkv, preferred_element_type=jnp.float32)
        mixed_heads = attend(projected, cosine_table[:, :, None], sine_table[:, :, None], window_tokens, HD)
        branch = jnp.zeros((tokens.shape[0], D), jnp.float32)
        for group in range(N_MP):
            group_term = jnp.dot(mixed_heads[:, group * groups:(group + 1) * groups], w_out[group * groups:(group + 1) * groups], preferred_element_type=jnp.float32)
            branch = branch + settle(group_term)
        block_out = (tokens.astype(jnp.float32) + branch).astype(jnp.bfloat16)
        source, live_rows = merge_source(heights[0], widths[0], slot_table[0], WS, WIN_CAP * window_tokens)
        picked = jnp.take(block_out, source, axis=0)
        return jnp.where(live_rows[:, None], picked, jnp.zeros_like(picked))
    blocks = lax.map(one_page, jnp.arange(PAGES, dtype=jnp.int32))
    return blocks.reshape(PAGES * WIN_CAP * window_tokens, D)
```

```python
import jax
import jax.numpy as jnp
from jax import lax
from jax.sharding import PartitionSpec as P

HD = 80
WS = 8
QUARTERS = 4


EPSILON = 1e-06


def angle_tables(row_place, column_place, head_size):
    quarter = head_size // 4
    frequency = 1.0 / 10000.0 ** (jnp.arange(quarter, dtype=jnp.float32) * 2.0 / (head_size // 2))
    angles = jnp.concatenate(
        [
            row_place[..., None].astype(jnp.float32) * frequency,
            column_place[..., None].astype(jnp.float32) * frequency,
        ],
        axis=-1,
    )
    angles = jnp.concatenate([angles, angles], axis=-1)
    return (jnp.cos(angles), jnp.sin(angles))


def slot_positions(page_widths, slot_table, slot_numbers, window_side):
    matches = slot_table[:, :, None] == slot_numbers[None, None, :]
    ordinal = jnp.arange(slot_table.shape[1], dtype=jnp.int32)
    window = jnp.sum(jnp.where(matches, ordinal[None, :, None], 0), axis=1)
    across = page_widths // window_side
    window_row = window // across[:, None]
    window_column = window % across[:, None]
    unit_side = window_side // 2
    position = jnp.arange(window_side * window_side, dtype=jnp.int32)
    merge_unit = position // 4
    corner = position % 4
    inner_row = merge_unit // unit_side * 2 + corner // 2
    inner_column = merge_unit % unit_side * 2 + corner % 2
    row_place = window_row[:, :, None] * window_side + inner_row
    column_place = window_column[:, :, None] * window_side + inner_column
    return (row_place, column_place)


def block_sources(height, page_width, slot_row, block_count):
    across = page_width // WS
    block = jnp.arange(block_count, dtype=jnp.int32)
    band = block // across
    column = block % across
    window_row = band // QUARTERS
    quarter = band % QUARTERS
    live = window_row < height // WS
    window = jnp.where(live, window_row * across + column, 0)
    ordinal = jnp.arange(slot_row.shape[0], dtype=jnp.int32)
    slot = jnp.sum(jnp.where(window[:, None] == ordinal[None, :], slot_row[None, :], 0), axis=1)
    return (slot * QUARTERS + quarter, live)


def normalize(block_in):
    values = block_in.astype(jnp.float32)
    factor = lax.rsqrt(jnp.mean(values * values, axis=-1, keepdims=True) + EPSILON)
    return (values * factor).astype(jnp.bfloat16)


def rotated_columns(weight):
    half = weight.shape[-1] // 2
    return jnp.concatenate([-weight[..., half:], weight[..., :half]], axis=-1)


def local(patches, w_qkv, w_out, page_rows, page_cols, window_slot):
    seq_index = lax.axis_index("seq")
    seq_count = lax.axis_size("seq")
    mp_index = lax.axis_index("mp")
    page_count = window_slot.shape[0]
    slot_count = window_slot.shape[1]
    slots_held = slot_count // seq_count
    window_tokens = WS * WS
    quarter_tokens = window_tokens // QUARTERS
    model_width = patches.shape[1]
    windows = patches.shape[0] // window_tokens

    joined = lax.all_gather(
        jnp.concatenate([w_qkv, w_out.T], axis=1), "seq", axis=0, tiled=True
    )
    qkv = joined[:, : w_qkv.shape[1]]
    out_rows_t = joined[:, w_qkv.shape[1] :]
    heads = qkv.shape[1] // (3 * HD)
    qkv = qkv.reshape(model_width, heads, 3, HD)
    w_q = qkv[:, :, 0]
    w_k = qkv[:, :, 1]
    w_v = qkv[:, :, 2].reshape(model_width, heads * HD)
    fused = jnp.concatenate(
        [
            w_q.reshape(model_width, heads * HD),
            w_k.reshape(model_width, heads * HD),
            rotated_columns(w_q).reshape(model_width, heads * HD),
            rotated_columns(w_k).reshape(model_width, heads * HD),
            w_v,
        ],
        axis=1,
    )
    out_full_t = lax.all_gather(out_rows_t, "mp", axis=1, tiled=True)

    slot_numbers = seq_index * slots_held + jnp.arange(slots_held, dtype=jnp.int32)
    row_place, column_place = slot_positions(page_cols, window_slot, slot_numbers, WS)
    cosine, sine = angle_tables(
        row_place.reshape(-1, window_tokens), column_place.reshape(-1, window_tokens), HD
    )
    cosine = jnp.tile(cosine.reshape(-1, HD), (1, 2 * heads))
    sine = jnp.tile(sine.reshape(-1, HD), (1, 2 * heads))

    normed = normalize(patches)
    projected = jnp.dot(normed, fused, preferred_element_type=jnp.float32)
    width = heads * HD
    turned = projected[:, : 2 * width] * cosine + projected[:, 2 * width : 4 * width] * sine
    turned = turned.astype(jnp.bfloat16).reshape(windows, window_tokens, 2 * width)
    queries = turned[:, :, :width]
    key_block = turned[:, :, width:]
    values = projected[:, 4 * width :].astype(jnp.bfloat16).reshape(windows, window_tokens, width)

    lane_head = jnp.arange(width, dtype=jnp.int32) // HD
    scale = 1.0 / (HD ** 0.5)
    mixed = jnp.zeros((windows, window_tokens, width), jnp.float32)
    for head in range(heads):
        mask = lane_head == head
        picked = jnp.where(mask, queries, jnp.zeros_like(queries))
        scores = jnp.einsum(
            "wqd,wkd->wqk", picked, key_block, preferred_element_type=jnp.float32
        ) * scale
        row_max = jnp.max(scores, axis=-1, keepdims=True)
        lifted = jnp.exp(scores - row_max)
        weights = (lifted / jnp.sum(lifted, axis=-1, keepdims=True)).astype(jnp.bfloat16)
        own_values = jnp.where(mask, values, jnp.zeros_like(values))
        mixed = mixed + jnp.einsum(
            "wqk,wkd->wqd", weights, own_values, preferred_element_type=jnp.float32
        )
    mixed = mixed.astype(jnp.bfloat16)

    spread = mixed.reshape(windows, QUARTERS, quarter_tokens, 1, width)
    gathered = lax.all_to_all(spread, "mp", split_axis=1, concat_axis=3, tiled=True)
    gathered = gathered.reshape(windows * quarter_tokens, QUARTERS * width)

    branch = lax.dot_general(
        gathered, out_full_t, (((1,), (1,)), ((), ())), preferred_element_type=jnp.float32
    )
    residual = patches.reshape(windows, QUARTERS, quarter_tokens, model_width)
    residual = lax.dynamic_index_in_dim(residual, mp_index, 1, keepdims=False)
    residual = residual.reshape(windows * quarter_tokens, model_width).astype(jnp.float32)
    block_out = (residual + branch).astype(jnp.bfloat16)

    share_width = model_width // QUARTERS
    sectioned = block_out.reshape(page_count, quarter_tokens, QUARTERS, share_width)
    sectioned = jnp.transpose(sectioned, (0, 2, 1, 3)).reshape(
        page_count * QUARTERS, quarter_tokens, share_width
    )
    landed = lax.all_to_all(sectioned, ("seq", "mp"), split_axis=0, concat_axis=0, tiled=True)

    own_pages = page_count // seq_count
    first_page = seq_index * own_pages
    heights = lax.dynamic_slice_in_dim(page_rows, first_page, own_pages, 0)
    widths = lax.dynamic_slice_in_dim(page_cols, first_page, own_pages, 0)
    slot_rows = lax.dynamic_slice_in_dim(window_slot, first_page, own_pages, 0)
    block_count = slot_count * QUARTERS // own_pages

    landed = landed.reshape(own_pages, block_count, quarter_tokens, share_width)

    def regroup(received, height, page_width, slot_row):
        source, live = block_sources(height, page_width, slot_row, block_count)
        picked = jnp.take(received, source, axis=0)
        return jnp.where(live[:, None, None], picked, jnp.zeros_like(picked))

    merged = jax.vmap(regroup)(landed, heights, widths, slot_rows)
    return merged.reshape(-1, share_width)


def solution(mesh):
    return jax.shard_map(
        local,
        mesh=mesh,
        in_specs=(P("seq", None), P("seq", "mp"), P("mp", "seq"), P(), P(), P()),
        out_specs=P("seq", "mp"),
        check_vma=False,
    )
```

```python
import jax
import jax.numpy as jnp
from jax import lax
from jax.sharding import PartitionSpec as P

HD = 80
WS = 8
QUARTERS = 4
HALVES = 2
SEQ_PARTS = ("z", "y", "core")


EPSILON = 1e-06


def angle_tables(row_place, column_place, head_size):
    quarter = head_size // 4
    frequency = 1.0 / 10000.0 ** (jnp.arange(quarter, dtype=jnp.float32) * 2.0 / (head_size // 2))
    angles = jnp.concatenate(
        [
            row_place[..., None].astype(jnp.float32) * frequency,
            column_place[..., None].astype(jnp.float32) * frequency,
        ],
        axis=-1,
    )
    angles = jnp.concatenate([angles, angles], axis=-1)
    return (jnp.cos(angles), jnp.sin(angles))


def slot_positions(page_widths, slot_table, slot_numbers, window_side):
    matches = slot_table[:, :, None] == slot_numbers[None, None, :]
    ordinal = jnp.arange(slot_table.shape[1], dtype=jnp.int32)
    window = jnp.sum(jnp.where(matches, ordinal[None, :, None], 0), axis=1)
    across = page_widths // window_side
    window_row = window // across[:, None]
    window_column = window % across[:, None]
    unit_side = window_side // 2
    position = jnp.arange(window_side * window_side, dtype=jnp.int32)
    merge_unit = position // 4
    corner = position % 4
    inner_row = merge_unit // unit_side * 2 + corner // 2
    inner_column = merge_unit % unit_side * 2 + corner % 2
    row_place = window_row[:, :, None] * window_side + inner_row
    column_place = window_column[:, :, None] * window_side + inner_column
    return (row_place, column_place)


def block_sources(height, page_width, slot_row, block_count):
    across = page_width // WS
    block = jnp.arange(block_count, dtype=jnp.int32)
    band = block // across
    column = block % across
    window_row = band // QUARTERS
    quarter = band % QUARTERS
    live = window_row < height // WS
    window = jnp.where(live, window_row * across + column, 0)
    ordinal = jnp.arange(slot_row.shape[0], dtype=jnp.int32)
    slot = jnp.sum(jnp.where(window[:, None] == ordinal[None, :], slot_row[None, :], 0), axis=1)
    return (slot * QUARTERS + quarter, live)


def normalize(block_in):
    values = block_in.astype(jnp.float32)
    factor = lax.rsqrt(jnp.mean(values * values, axis=-1, keepdims=True) + EPSILON)
    return (values * factor).astype(jnp.bfloat16)


def rotated_columns(weight):
    half = weight.shape[-1] // 2
    return jnp.concatenate([-weight[..., half:], weight[..., :half]], axis=-1)


def local(patches, w_qkv, w_out, page_rows, page_cols, window_slot):
    seq_index = lax.axis_index(SEQ_PARTS)
    seq_count = lax.axis_size(SEQ_PARTS)
    mp_index = lax.axis_index("mp")
    page_count = window_slot.shape[0]
    slot_count = window_slot.shape[1]
    slots_held = slot_count // seq_count
    window_tokens = WS * WS
    quarter_tokens = window_tokens // QUARTERS
    model_width = patches.shape[1]
    windows = patches.shape[0] // window_tokens

    joined = jnp.concatenate([w_qkv, w_out.T], axis=1)
    for name in SEQ_PARTS:
        joined = lax.all_gather(joined, name, axis=0)
    part_sizes = [lax.axis_size(name) for name in SEQ_PARTS]
    joined = joined.reshape(*reversed(part_sizes), *joined.shape[-2:])
    joined = jnp.transpose(joined, (*reversed(range(len(SEQ_PARTS))), len(SEQ_PARTS), len(SEQ_PARTS) + 1))
    joined = joined.reshape(-1, joined.shape[-1])
    qkv = joined[:, : w_qkv.shape[1]]
    out_rows_t = joined[:, w_qkv.shape[1] :]
    heads = qkv.shape[1] // (3 * HD)
    qkv = qkv.reshape(model_width, heads, 3, HD)
    w_q = qkv[:, :, 0]
    w_k = qkv[:, :, 1]
    w_v = qkv[:, :, 2].reshape(model_width, heads * HD)
    fused = jnp.concatenate(
        [
            w_q.reshape(model_width, heads * HD),
            w_k.reshape(model_width, heads * HD),
            rotated_columns(w_q).reshape(model_width, heads * HD),
            rotated_columns(w_k).reshape(model_width, heads * HD),
            w_v,
        ],
        axis=1,
    )
    out_full_t = lax.all_gather(out_rows_t, "mp", axis=1, tiled=True)

    slot_numbers = seq_index * slots_held + jnp.arange(slots_held, dtype=jnp.int32)
    row_place, column_place = slot_positions(page_cols, window_slot, slot_numbers, WS)
    cosine, sine = angle_tables(
        row_place.reshape(-1, window_tokens), column_place.reshape(-1, window_tokens), HD
    )
    cosine = jnp.tile(cosine.reshape(-1, HD), (1, 2 * heads))
    sine = jnp.tile(sine.reshape(-1, HD), (1, 2 * heads))

    normed = normalize(patches)
    projected = jnp.dot(normed, fused, preferred_element_type=jnp.float32)
    width = heads * HD
    turned = projected[:, : 2 * width] * cosine + projected[:, 2 * width : 4 * width] * sine
    turned = turned.astype(jnp.bfloat16).reshape(windows, window_tokens, 2 * width)
    queries = turned[:, :, :width]
    key_block = turned[:, :, width:]
    values = projected[:, 4 * width :].astype(jnp.bfloat16).reshape(windows, window_tokens, width)

    lane_head = jnp.arange(width, dtype=jnp.int32) // HD
    scale = 1.0 / (HD ** 0.5)
    share_width = model_width // QUARTERS
    half_tokens = quarter_tokens // HALVES
    split_queries = queries.reshape(windows, QUARTERS, HALVES, half_tokens, width)
    residual_all = patches.reshape(windows, QUARTERS, HALVES, half_tokens, model_width)
    residual_all = lax.dynamic_index_in_dim(residual_all, mp_index, 1, keepdims=False)
    landed_halves = []
    for half in range(HALVES):
        own_queries = split_queries[:, :, half].reshape(windows, QUARTERS * half_tokens, width)
        mixed = jnp.zeros((windows, QUARTERS * half_tokens, width), jnp.float32)
        for head in range(heads):
            mask = lane_head == head
            picked = jnp.where(mask, own_queries, jnp.zeros_like(own_queries))
            scores = jnp.einsum(
                "wqd,wkd->wqk", picked, key_block, preferred_element_type=jnp.float32
            ) * scale
            row_max = jnp.max(scores, axis=-1, keepdims=True)
            lifted = jnp.exp(scores - row_max)
            weights = (lifted / jnp.sum(lifted, axis=-1, keepdims=True)).astype(jnp.bfloat16)
            own_values = jnp.where(mask, values, jnp.zeros_like(values))
            mixed = mixed + jnp.einsum(
                "wqk,wkd->wqd", weights, own_values, preferred_element_type=jnp.float32
            )
        mixed = mixed.astype(jnp.bfloat16)

        spread = mixed.reshape(windows, QUARTERS, half_tokens, 1, width)
        gathered = lax.all_to_all(spread, "mp", split_axis=1, concat_axis=3, tiled=True)
        gathered = gathered.reshape(windows * half_tokens, QUARTERS * width)

        branch = lax.dot_general(
            gathered, out_full_t, (((1,), (1,)), ((), ())), preferred_element_type=jnp.float32
        )
        residual = residual_all[:, half].reshape(windows * half_tokens, model_width)
        block_out = (residual.astype(jnp.float32) + branch).astype(jnp.bfloat16)

        sectioned = block_out.reshape(page_count, half_tokens, QUARTERS, share_width)
        sectioned = jnp.transpose(sectioned, (0, 2, 1, 3)).reshape(
            page_count * QUARTERS, half_tokens, share_width
        )
        landed_halves.append(
            lax.all_to_all(sectioned, (*SEQ_PARTS, "mp"), split_axis=0, concat_axis=0, tiled=True)
        )
    landed = jnp.concatenate(landed_halves, axis=1)

    own_pages = page_count // seq_count
    first_page = seq_index * own_pages
    heights = lax.dynamic_slice_in_dim(page_rows, first_page, own_pages, 0)
    widths = lax.dynamic_slice_in_dim(page_cols, first_page, own_pages, 0)
    slot_rows = lax.dynamic_slice_in_dim(window_slot, first_page, own_pages, 0)
    block_count = slot_count * QUARTERS // own_pages

    landed = landed.reshape(own_pages, block_count, quarter_tokens, share_width)

    def regroup(received, height, page_width, slot_row):
        source, live = block_sources(height, page_width, slot_row, block_count)
        picked = jnp.take(received, source, axis=0)
        return jnp.where(live[:, None, None], picked, jnp.zeros_like(picked))

    merged = jax.vmap(regroup)(landed, heights, widths, slot_rows)
    return merged.reshape(-1, share_width)


def solution(mesh):
    seq_devices = mesh.devices[:, 0]
    part_sizes = (
        len({d.coords[2] for d in seq_devices}),
        len({d.coords[1] for d in seq_devices}),
        len({d.core_on_chip for d in seq_devices}),
    )
    fine = jax.sharding.Mesh(
        mesh.devices.reshape(*part_sizes, mesh.devices.shape[1]), (*SEQ_PARTS, "mp")
    )
    return jax.shard_map(
        local,
        mesh=fine,
        in_specs=(P(SEQ_PARTS, None), P(SEQ_PARTS, "mp"), P("mp", SEQ_PARTS), P(), P(), P()),
        out_specs=P(SEQ_PARTS, "mp"),
        check_vma=False,
    )
```

```python
import jax
import jax.numpy as jnp
from jax import lax
from jax.sharding import PartitionSpec as P

HD = 80
WS = 8
QUARTERS = 4


EPSILON = 1e-06


def angle_tables(row_place, column_place, head_size):
    quarter = head_size // 4
    frequency = 1.0 / 10000.0 ** (jnp.arange(quarter, dtype=jnp.float32) * 2.0 / (head_size // 2))
    angles = jnp.concatenate(
        [
            row_place[..., None].astype(jnp.float32) * frequency,
            column_place[..., None].astype(jnp.float32) * frequency,
        ],
        axis=-1,
    )
    angles = jnp.concatenate([angles, angles], axis=-1)
    return (jnp.cos(angles), jnp.sin(angles))


def slot_positions(page_widths, slot_table, slot_numbers, window_side):
    matches = slot_table[:, :, None] == slot_numbers[None, None, :]
    ordinal = jnp.arange(slot_table.shape[1], dtype=jnp.int32)
    window = jnp.sum(jnp.where(matches, ordinal[None, :, None], 0), axis=1)
    across = page_widths // window_side
    window_row = window // across[:, None]
    window_column = window % across[:, None]
    unit_side = window_side // 2
    position = jnp.arange(window_side * window_side, dtype=jnp.int32)
    merge_unit = position // 4
    corner = position % 4
    inner_row = merge_unit // unit_side * 2 + corner // 2
    inner_column = merge_unit % unit_side * 2 + corner % 2
    row_place = window_row[:, :, None] * window_side + inner_row
    column_place = window_column[:, :, None] * window_side + inner_column
    return (row_place, column_place)


def block_sources(height, page_width, slot_row, block_count):
    across = page_width // WS
    block = jnp.arange(block_count, dtype=jnp.int32)
    band = block // across
    column = block % across
    window_row = band // QUARTERS
    quarter = band % QUARTERS
    live = window_row < height // WS
    window = jnp.where(live, window_row * across + column, 0)
    ordinal = jnp.arange(slot_row.shape[0], dtype=jnp.int32)
    slot = jnp.sum(jnp.where(window[:, None] == ordinal[None, :], slot_row[None, :], 0), axis=1)
    return (slot * QUARTERS + quarter, live)


def normalize(block_in):
    values = block_in.astype(jnp.float32)
    factor = lax.rsqrt(jnp.mean(values * values, axis=-1, keepdims=True) + EPSILON)
    return (values * factor).astype(jnp.bfloat16)


def rotated_columns(weight):
    half = weight.shape[-1] // 2
    return jnp.concatenate([-weight[..., half:], weight[..., :half]], axis=-1)


def local(patches, w_qkv, w_out, page_rows, page_cols, window_slot):
    seq_index = lax.axis_index("seq")
    seq_count = lax.axis_size("seq")
    mp_index = lax.axis_index("mp")
    page_count = window_slot.shape[0]
    slot_count = window_slot.shape[1]
    slots_held = slot_count // seq_count
    window_tokens = WS * WS
    quarter_tokens = window_tokens // QUARTERS
    model_width = patches.shape[1]
    windows = patches.shape[0] // window_tokens

    joined = lax.all_gather(
        jnp.concatenate([w_qkv, w_out.T], axis=1), "seq", axis=0, tiled=True
    )
    qkv = joined[:, : w_qkv.shape[1]]
    out_rows_t = joined[:, w_qkv.shape[1] :]
    heads = qkv.shape[1] // (3 * HD)
    qkv = qkv.reshape(model_width, heads, 3, HD)
    w_q = qkv[:, :, 0]
    w_k = qkv[:, :, 1]
    w_v = qkv[:, :, 2].reshape(model_width, heads * HD)
    fused = jnp.concatenate(
        [
            w_q.reshape(model_width, heads * HD),
            w_k.reshape(model_width, heads * HD),
            rotated_columns(w_q).reshape(model_width, heads * HD),
            rotated_columns(w_k).reshape(model_width, heads * HD),
            w_v,
        ],
        axis=1,
    )
    out_full_t = lax.all_gather(out_rows_t, "mp", axis=1, tiled=True)

    slot_numbers = seq_index * slots_held + jnp.arange(slots_held, dtype=jnp.int32)
    row_place, column_place = slot_positions(page_cols, window_slot, slot_numbers, WS)
    cosine, sine = angle_tables(
        row_place.reshape(-1, window_tokens), column_place.reshape(-1, window_tokens), HD
    )
    cosine = jnp.tile(cosine.reshape(-1, HD), (1, 2 * heads))
    sine = jnp.tile(sine.reshape(-1, HD), (1, 2 * heads))

    normed = normalize(patches)
    projected = jnp.dot(normed, fused, preferred_element_type=jnp.float32)
    width = heads * HD
    turned = projected[:, : 2 * width] * cosine + projected[:, 2 * width : 4 * width] * sine
    turned = turned.astype(jnp.bfloat16).reshape(windows, window_tokens, 2 * width)
    queries = turned[:, :, :width]
    key_block = turned[:, :, width:]
    values = projected[:, 4 * width :].astype(jnp.bfloat16).reshape(windows, window_tokens, width)

    lane_head = jnp.arange(width, dtype=jnp.int32) // HD
    head_mask = (jnp.arange(heads, dtype=jnp.int32)[:, None] == lane_head[None, :])[None, :, None, :]
    spread_keys = jnp.where(head_mask, key_block[:, None], jnp.zeros_like(key_block[:, None]))
    spread_keys = spread_keys.reshape(windows, heads * window_tokens, width)
    spread_values = jnp.where(head_mask, values[:, None], jnp.zeros_like(values[:, None]))
    spread_values = spread_values.reshape(windows, heads * window_tokens, width)
    scale = 1.0 / (HD ** 0.5)
    scores = jnp.einsum(
        "wqd,wkd->wqk", queries, spread_keys, preferred_element_type=jnp.float32
    ) * scale
    scores = scores.reshape(windows, window_tokens, heads, window_tokens)
    row_max = jnp.max(scores, axis=-1, keepdims=True)
    lifted = jnp.exp(scores - row_max)
    weights = (lifted / jnp.sum(lifted, axis=-1, keepdims=True)).astype(jnp.bfloat16)
    weights = weights.reshape(windows, window_tokens, heads * window_tokens)
    mixed = jnp.einsum(
        "wqk,wkd->wqd", weights, spread_values, preferred_element_type=jnp.float32
    )
    mixed = mixed.astype(jnp.bfloat16)

    spread = mixed.reshape(windows, QUARTERS, quarter_tokens, 1, width)
    gathered = lax.all_to_all(spread, "mp", split_axis=1, concat_axis=3, tiled=True)
    gathered = gathered.reshape(windows * quarter_tokens, QUARTERS * width)

    branch = lax.dot_general(
        gathered, out_full_t, (((1,), (1,)), ((), ())), preferred_element_type=jnp.float32
    )
    residual = patches.reshape(windows, QUARTERS, quarter_tokens, model_width)
    residual = lax.dynamic_index_in_dim(residual, mp_index, 1, keepdims=False)
    residual = residual.reshape(windows * quarter_tokens, model_width).astype(jnp.float32)
    block_out = (residual + branch).astype(jnp.bfloat16)

    share_width = model_width // QUARTERS
    sectioned = block_out.reshape(page_count, quarter_tokens, QUARTERS, share_width)
    sectioned = jnp.transpose(sectioned, (0, 2, 1, 3)).reshape(
        page_count * QUARTERS, quarter_tokens, share_width
    )
    landed = lax.all_to_all(sectioned, ("seq", "mp"), split_axis=0, concat_axis=0, tiled=True)

    own_pages = page_count // seq_count
    first_page = seq_index * own_pages
    heights = lax.dynamic_slice_in_dim(page_rows, first_page, own_pages, 0)
    widths = lax.dynamic_slice_in_dim(page_cols, first_page, own_pages, 0)
    slot_rows = lax.dynamic_slice_in_dim(window_slot, first_page, own_pages, 0)
    block_count = slot_count * QUARTERS // own_pages

    landed = landed.reshape(own_pages, block_count, quarter_tokens, share_width)

    def regroup(received, height, page_width, slot_row):
        source, live = block_sources(height, page_width, slot_row, block_count)
        picked = jnp.take(received, source, axis=0)
        return jnp.where(live[:, None, None], picked, jnp.zeros_like(picked))

    merged = jax.vmap(regroup)(landed, heights, widths, slot_rows)
    return merged.reshape(-1, share_width)


def solution(mesh):
    return jax.shard_map(
        local,
        mesh=mesh,
        in_specs=(P("seq", None), P("seq", "mp"), P("mp", "seq"), P(), P(), P()),
        out_specs=P("seq", "mp"),
        check_vma=False,
    )
```

```python
import jax
import jax.numpy as jnp
from jax import lax
from jax.sharding import PartitionSpec as P

HD = 80
WS = 8
QUARTERS = 4


EPSILON = 1e-06


def angle_tables(row_place, column_place, head_size):
    quarter = head_size // 4
    frequency = 1.0 / 10000.0 ** (jnp.arange(quarter, dtype=jnp.float32) * 2.0 / (head_size // 2))
    angles = jnp.concatenate(
        [
            row_place[..., None].astype(jnp.float32) * frequency,
            column_place[..., None].astype(jnp.float32) * frequency,
        ],
        axis=-1,
    )
    angles = jnp.concatenate([angles, angles], axis=-1)
    return (jnp.cos(angles), jnp.sin(angles))


def slot_positions(page_widths, slot_table, slot_numbers, window_side):
    matches = slot_table[:, :, None] == slot_numbers[None, None, :]
    ordinal = jnp.arange(slot_table.shape[1], dtype=jnp.int32)
    window = jnp.sum(jnp.where(matches, ordinal[None, :, None], 0), axis=1)
    across = page_widths // window_side
    window_row = window // across[:, None]
    window_column = window % across[:, None]
    unit_side = window_side // 2
    position = jnp.arange(window_side * window_side, dtype=jnp.int32)
    merge_unit = position // 4
    corner = position % 4
    inner_row = merge_unit // unit_side * 2 + corner // 2
    inner_column = merge_unit % unit_side * 2 + corner % 2
    row_place = window_row[:, :, None] * window_side + inner_row
    column_place = window_column[:, :, None] * window_side + inner_column
    return (row_place, column_place)


def block_sources(height, page_width, slot_row, block_count):
    across = page_width // WS
    block = jnp.arange(block_count, dtype=jnp.int32)
    band = block // across
    column = block % across
    window_row = band // QUARTERS
    quarter = band % QUARTERS
    live = window_row < height // WS
    window = jnp.where(live, window_row * across + column, 0)
    ordinal = jnp.arange(slot_row.shape[0], dtype=jnp.int32)
    slot = jnp.sum(jnp.where(window[:, None] == ordinal[None, :], slot_row[None, :], 0), axis=1)
    return (slot * QUARTERS + quarter, live)


def normalize(block_in):
    values = block_in.astype(jnp.float32)
    factor = lax.rsqrt(jnp.mean(values * values, axis=-1, keepdims=True) + EPSILON)
    return (values * factor).astype(jnp.bfloat16)


def rotated_columns(weight):
    half = weight.shape[-1] // 2
    return jnp.concatenate([-weight[..., half:], weight[..., :half]], axis=-1)


def local(patches, w_qkv, w_out, page_rows, page_cols, window_slot):
    seq_index = lax.axis_index("seq")
    seq_count = lax.axis_size("seq")
    mp_index = lax.axis_index("mp")
    page_count = window_slot.shape[0]
    slot_count = window_slot.shape[1]
    slots_held = slot_count // seq_count
    window_tokens = WS * WS
    quarter_tokens = window_tokens // QUARTERS
    model_width = patches.shape[1]
    windows = patches.shape[0] // window_tokens

    own = jnp.concatenate([w_qkv, w_out.T], axis=1)
    placed = jnp.zeros((seq_count, *own.shape), own.dtype)
    placed = lax.dynamic_update_index_in_dim(placed, own, seq_index, 0)
    joined = lax.psum(placed, "seq").reshape(-1, own.shape[1])
    qkv = joined[:, : w_qkv.shape[1]]
    out_rows_t = joined[:, w_qkv.shape[1] :]
    heads = qkv.shape[1] // (3 * HD)
    qkv = qkv.reshape(model_width, heads, 3, HD)
    w_q = qkv[:, :, 0]
    w_k = qkv[:, :, 1]
    w_v = qkv[:, :, 2].reshape(model_width, heads * HD)
    fused = jnp.concatenate(
        [
            w_q.reshape(model_width, heads * HD),
            w_k.reshape(model_width, heads * HD),
            rotated_columns(w_q).reshape(model_width, heads * HD),
            rotated_columns(w_k).reshape(model_width, heads * HD),
            w_v,
        ],
        axis=1,
    )
    out_full_t = lax.all_gather(out_rows_t, "mp", axis=1, tiled=True)

    slot_numbers = seq_index * slots_held + jnp.arange(slots_held, dtype=jnp.int32)
    row_place, column_place = slot_positions(page_cols, window_slot, slot_numbers, WS)
    cosine, sine = angle_tables(
        row_place.reshape(-1, window_tokens), column_place.reshape(-1, window_tokens), HD
    )
    cosine = jnp.tile(cosine.reshape(-1, HD), (1, 2 * heads))
    sine = jnp.tile(sine.reshape(-1, HD), (1, 2 * heads))

    normed = normalize(patches)
    projected = jnp.dot(normed, fused, preferred_element_type=jnp.float32)
    width = heads * HD
    turned = projected[:, : 2 * width] * cosine + projected[:, 2 * width : 4 * width] * sine
    turned = turned.astype(jnp.bfloat16).reshape(windows, window_tokens, 2 * width)
    queries = turned[:, :, :width]
    key_block = turned[:, :, width:]
    values = projected[:, 4 * width :].astype(jnp.bfloat16).reshape(windows, window_tokens, width)

    lane_head = jnp.arange(width, dtype=jnp.int32) // HD
    scale = 1.0 / (HD ** 0.5)
    mixed = jnp.zeros((windows, window_tokens, width), jnp.float32)
    for head in range(heads):
        mask = lane_head == head
        picked = jnp.where(mask, queries, jnp.zeros_like(queries))
        scores = jnp.einsum(
            "wqd,wkd->wqk", picked, key_block, preferred_element_type=jnp.float32
        ) * scale
        row_max = jnp.max(scores, axis=-1, keepdims=True)
        lifted = jnp.exp(scores - row_max)
        weights = (lifted / jnp.sum(lifted, axis=-1, keepdims=True)).astype(jnp.bfloat16)
        own_values = jnp.where(mask, values, jnp.zeros_like(values))
        mixed = mixed + jnp.einsum(
            "wqk,wkd->wqd", weights, own_values, preferred_element_type=jnp.float32
        )
    mixed = mixed.astype(jnp.bfloat16)

    spread = mixed.reshape(windows, QUARTERS, quarter_tokens, 1, width)
    gathered = lax.all_to_all(spread, "mp", split_axis=1, concat_axis=3, tiled=True)
    gathered = gathered.reshape(windows * quarter_tokens, QUARTERS * width)

    branch = lax.dot_general(
        gathered, out_full_t, (((1,), (1,)), ((), ())), preferred_element_type=jnp.float32
    )
    residual = patches.reshape(windows, QUARTERS, quarter_tokens, model_width)
    residual = lax.dynamic_index_in_dim(residual, mp_index, 1, keepdims=False)
    residual = residual.reshape(windows * quarter_tokens, model_width).astype(jnp.float32)
    block_out = (residual + branch).astype(jnp.bfloat16)

    share_width = model_width // QUARTERS
    sectioned = block_out.reshape(page_count, quarter_tokens, QUARTERS, share_width)
    sectioned = jnp.transpose(sectioned, (0, 2, 1, 3)).reshape(
        page_count * QUARTERS, quarter_tokens, share_width
    )
    landed = lax.all_to_all(sectioned, ("seq", "mp"), split_axis=0, concat_axis=0, tiled=True)

    own_pages = page_count // seq_count
    first_page = seq_index * own_pages
    heights = lax.dynamic_slice_in_dim(page_rows, first_page, own_pages, 0)
    widths = lax.dynamic_slice_in_dim(page_cols, first_page, own_pages, 0)
    slot_rows = lax.dynamic_slice_in_dim(window_slot, first_page, own_pages, 0)
    block_count = slot_count * QUARTERS // own_pages

    landed = landed.reshape(own_pages, block_count, quarter_tokens, share_width)

    def regroup(received, height, page_width, slot_row):
        source, live = block_sources(height, page_width, slot_row, block_count)
        picked = jnp.take(received, source, axis=0)
        return jnp.where(live[:, None, None], picked, jnp.zeros_like(picked))

    merged = jax.vmap(regroup)(landed, heights, widths, slot_rows)
    return merged.reshape(-1, share_width)


def solution(mesh):
    return jax.shard_map(
        local,
        mesh=mesh,
        in_specs=(P("seq", None), P("seq", "mp"), P("mp", "seq"), P(), P(), P()),
        out_specs=P("seq", "mp"),
        check_vma=False,
    )
```

```python
import jax
import jax.numpy as jnp
from jax import lax
from jax.sharding import PartitionSpec as P

HD = 80
WS = 8
QUARTERS = 4


EPSILON = 1e-06


def angle_tables(row_place, column_place, head_size):
    quarter = head_size // 4
    frequency = 1.0 / 10000.0 ** (jnp.arange(quarter, dtype=jnp.float32) * 2.0 / (head_size // 2))
    angles = jnp.concatenate(
        [
            row_place[..., None].astype(jnp.float32) * frequency,
            column_place[..., None].astype(jnp.float32) * frequency,
        ],
        axis=-1,
    )
    angles = jnp.concatenate([angles, angles], axis=-1)
    return (jnp.cos(angles), jnp.sin(angles))


def slot_positions(page_widths, slot_table, slot_numbers, window_side):
    matches = slot_table[:, :, None] == slot_numbers[None, None, :]
    ordinal = jnp.arange(slot_table.shape[1], dtype=jnp.int32)
    window = jnp.sum(jnp.where(matches, ordinal[None, :, None], 0), axis=1)
    across = page_widths // window_side
    window_row = window // across[:, None]
    window_column = window % across[:, None]
    unit_side = window_side // 2
    position = jnp.arange(window_side * window_side, dtype=jnp.int32)
    merge_unit = position // 4
    corner = position % 4
    inner_row = merge_unit // unit_side * 2 + corner // 2
    inner_column = merge_unit % unit_side * 2 + corner % 2
    row_place = window_row[:, :, None] * window_side + inner_row
    column_place = window_column[:, :, None] * window_side + inner_column
    return (row_place, column_place)


def block_sources(height, page_width, slot_row, block_count):
    across = page_width // WS
    block = jnp.arange(block_count, dtype=jnp.int32)
    band = block // across
    column = block % across
    window_row = band // QUARTERS
    quarter = band % QUARTERS
    live = window_row < height // WS
    window = jnp.where(live, window_row * across + column, 0)
    ordinal = jnp.arange(slot_row.shape[0], dtype=jnp.int32)
    slot = jnp.sum(jnp.where(window[:, None] == ordinal[None, :], slot_row[None, :], 0), axis=1)
    return (slot * QUARTERS + quarter, live)


def normalize(block_in):
    values = block_in.astype(jnp.float32)
    factor = lax.rsqrt(jnp.mean(values * values, axis=-1, keepdims=True) + EPSILON)
    return (values * factor).astype(jnp.bfloat16)


def rotated_columns(weight):
    half = weight.shape[-1] // 2
    return jnp.concatenate([-weight[..., half:], weight[..., :half]], axis=-1)


def local(patches, w_qkv, w_out, page_rows, page_cols, window_slot):
    seq_index = lax.axis_index("seq")
    seq_count = lax.axis_size("seq")
    mp_index = lax.axis_index("mp")
    page_count = window_slot.shape[0]
    slot_count = window_slot.shape[1]
    slots_held = slot_count // seq_count
    window_tokens = WS * WS
    quarter_tokens = window_tokens // QUARTERS
    model_width = patches.shape[1]
    windows = patches.shape[0] // window_tokens

    own_rows = w_qkv.shape[0]
    heads = w_qkv.shape[1] // (3 * HD)
    qkv = w_qkv.reshape(own_rows, heads, 3, HD)
    w_q = qkv[:, :, 0]
    w_k = qkv[:, :, 1]
    fused_rows = jnp.concatenate(
        [
            w_q.reshape(own_rows, heads * HD),
            w_k.reshape(own_rows, heads * HD),
            rotated_columns(w_q).reshape(own_rows, heads * HD),
            rotated_columns(w_k).reshape(own_rows, heads * HD),
            qkv[:, :, 2].reshape(own_rows, heads * HD),
            w_out.T,
        ],
        axis=1,
    )
    joined = lax.all_gather(fused_rows, "seq", axis=0, tiled=True)
    fused = joined[:, : 5 * heads * HD]
    out_rows_t = joined[:, 5 * heads * HD :]
    out_full_t = lax.all_gather(out_rows_t, "mp", axis=1, tiled=True)

    slot_numbers = seq_index * slots_held + jnp.arange(slots_held, dtype=jnp.int32)
    row_place, column_place = slot_positions(page_cols, window_slot, slot_numbers, WS)
    cosine, sine = angle_tables(
        row_place.reshape(-1, window_tokens), column_place.reshape(-1, window_tokens), HD
    )
    cosine = jnp.tile(cosine.reshape(-1, HD), (1, 2 * heads))
    sine = jnp.tile(sine.reshape(-1, HD), (1, 2 * heads))

    normed = normalize(patches)
    projected = jnp.dot(normed, fused, preferred_element_type=jnp.float32)
    width = heads * HD
    turned = projected[:, : 2 * width] * cosine + projected[:, 2 * width : 4 * width] * sine
    turned = turned.astype(jnp.bfloat16).reshape(windows, window_tokens, 2 * width)
    queries = turned[:, :, :width]
    key_block = turned[:, :, width:]
    values = projected[:, 4 * width :].astype(jnp.bfloat16).reshape(windows, window_tokens, width)

    lane_head = jnp.arange(width, dtype=jnp.int32) // HD
    scale = 1.0 / (HD ** 0.5)
    mixed = jnp.zeros((windows, window_tokens, width), jnp.float32)
    for head in range(heads):
        mask = lane_head == head
        picked = jnp.where(mask, queries, jnp.zeros_like(queries))
        scores = jnp.einsum(
            "wqd,wkd->wqk", picked, key_block, preferred_element_type=jnp.float32
        ) * scale
        row_max = jnp.max(scores, axis=-1, keepdims=True)
        lifted = jnp.exp(scores - row_max)
        weights = (lifted / jnp.sum(lifted, axis=-1, keepdims=True)).astype(jnp.bfloat16)
        own_values = jnp.where(mask, values, jnp.zeros_like(values))
        mixed = mixed + jnp.einsum(
            "wqk,wkd->wqd", weights, own_values, preferred_element_type=jnp.float32
        )
    mixed = mixed.astype(jnp.bfloat16)

    spread = mixed.reshape(windows, QUARTERS, quarter_tokens, 1, width)
    gathered = lax.all_to_all(spread, "mp", split_axis=1, concat_axis=3, tiled=True)
    gathered = gathered.reshape(windows * quarter_tokens, QUARTERS * width)

    branch = lax.dot_general(
        gathered, out_full_t, (((1,), (1,)), ((), ())), preferred_element_type=jnp.float32
    )
    residual = patches.reshape(windows, QUARTERS, quarter_tokens, model_width)
    residual = lax.dynamic_index_in_dim(residual, mp_index, 1, keepdims=False)
    residual = residual.reshape(windows * quarter_tokens, model_width).astype(jnp.float32)
    block_out = (residual + branch).astype(jnp.bfloat16)

    share_width = model_width // QUARTERS
    sectioned = block_out.reshape(page_count, quarter_tokens, QUARTERS, share_width)
    sectioned = jnp.transpose(sectioned, (0, 2, 1, 3)).reshape(
        page_count * QUARTERS, quarter_tokens, share_width
    )
    landed = lax.all_to_all(sectioned, ("seq", "mp"), split_axis=0, concat_axis=0, tiled=True)

    own_pages = page_count // seq_count
    first_page = seq_index * own_pages
    heights = lax.dynamic_slice_in_dim(page_rows, first_page, own_pages, 0)
    widths = lax.dynamic_slice_in_dim(page_cols, first_page, own_pages, 0)
    slot_rows = lax.dynamic_slice_in_dim(window_slot, first_page, own_pages, 0)
    block_count = slot_count * QUARTERS // own_pages

    landed = landed.reshape(own_pages, block_count, quarter_tokens, share_width)

    def regroup(received, height, page_width, slot_row):
        source, live = block_sources(height, page_width, slot_row, block_count)
        picked = jnp.take(received, source, axis=0)
        return jnp.where(live[:, None, None], picked, jnp.zeros_like(picked))

    merged = jax.vmap(regroup)(landed, heights, widths, slot_rows)
    return merged.reshape(-1, share_width)


def solution(mesh):
    return jax.shard_map(
        local,
        mesh=mesh,
        in_specs=(P("seq", None), P("seq", "mp"), P("mp", "seq"), P(), P(), P()),
        out_specs=P("seq", "mp"),
        check_vma=False,
    )
```

```python
import jax
import jax.numpy as jnp
from jax import lax
from jax.sharding import PartitionSpec as P

HD = 80
WS = 8
QUARTERS = 4
WINDOW_SETS = 2


EPSILON = 1e-06


def angle_tables(row_place, column_place, head_size):
    quarter = head_size // 4
    frequency = 1.0 / 10000.0 ** (jnp.arange(quarter, dtype=jnp.float32) * 2.0 / (head_size // 2))
    angles = jnp.concatenate(
        [
            row_place[..., None].astype(jnp.float32) * frequency,
            column_place[..., None].astype(jnp.float32) * frequency,
        ],
        axis=-1,
    )
    angles = jnp.concatenate([angles, angles], axis=-1)
    return (jnp.cos(angles), jnp.sin(angles))


def slot_positions(page_widths, slot_table, slot_numbers, window_side):
    matches = slot_table[:, :, None] == slot_numbers[None, None, :]
    ordinal = jnp.arange(slot_table.shape[1], dtype=jnp.int32)
    window = jnp.sum(jnp.where(matches, ordinal[None, :, None], 0), axis=1)
    across = page_widths // window_side
    window_row = window // across[:, None]
    window_column = window % across[:, None]
    unit_side = window_side // 2
    position = jnp.arange(window_side * window_side, dtype=jnp.int32)
    merge_unit = position // 4
    corner = position % 4
    inner_row = merge_unit // unit_side * 2 + corner // 2
    inner_column = merge_unit % unit_side * 2 + corner % 2
    row_place = window_row[:, :, None] * window_side + inner_row
    column_place = window_column[:, :, None] * window_side + inner_column
    return (row_place, column_place)


def block_sources(height, page_width, slot_row, block_count):
    across = page_width // WS
    block = jnp.arange(block_count, dtype=jnp.int32)
    band = block // across
    column = block % across
    window_row = band // QUARTERS
    quarter = band % QUARTERS
    live = window_row < height // WS
    window = jnp.where(live, window_row * across + column, 0)
    ordinal = jnp.arange(slot_row.shape[0], dtype=jnp.int32)
    slot = jnp.sum(jnp.where(window[:, None] == ordinal[None, :], slot_row[None, :], 0), axis=1)
    return (slot * QUARTERS + quarter, live)


def normalize(block_in):
    values = block_in.astype(jnp.float32)
    factor = lax.rsqrt(jnp.mean(values * values, axis=-1, keepdims=True) + EPSILON)
    return (values * factor).astype(jnp.bfloat16)


def rotated_columns(weight):
    half = weight.shape[-1] // 2
    return jnp.concatenate([-weight[..., half:], weight[..., :half]], axis=-1)


def local(patches, w_qkv, w_out, page_rows, page_cols, window_slot):
    seq_index = lax.axis_index("seq")
    seq_count = lax.axis_size("seq")
    mp_index = lax.axis_index("mp")
    page_count = window_slot.shape[0]
    slot_count = window_slot.shape[1]
    slots_held = slot_count // seq_count
    window_tokens = WS * WS
    quarter_tokens = window_tokens // QUARTERS
    model_width = patches.shape[1]
    windows = patches.shape[0] // window_tokens

    own_rows = w_qkv.shape[0]
    heads = w_qkv.shape[1] // (3 * HD)
    qkv = w_qkv.reshape(own_rows, heads, 3, HD)
    w_q = qkv[:, :, 0]
    w_k = qkv[:, :, 1]
    fused_rows = jnp.concatenate(
        [
            w_q.reshape(own_rows, heads * HD),
            w_k.reshape(own_rows, heads * HD),
            rotated_columns(w_q).reshape(own_rows, heads * HD),
            rotated_columns(w_k).reshape(own_rows, heads * HD),
            qkv[:, :, 2].reshape(own_rows, heads * HD),
            w_out.T,
        ],
        axis=1,
    )
    joined = lax.all_gather(fused_rows, "seq", axis=0, tiled=True)
    fused = joined[:, : 5 * heads * HD]
    out_rows_t = joined[:, 5 * heads * HD :]
    out_full_t = lax.all_gather(out_rows_t, "mp", axis=1, tiled=True)

    slot_numbers = seq_index * slots_held + jnp.arange(slots_held, dtype=jnp.int32)
    row_place, column_place = slot_positions(page_cols, window_slot, slot_numbers, WS)
    cosine, sine = angle_tables(
        row_place.reshape(-1, window_tokens), column_place.reshape(-1, window_tokens), HD
    )
    cosine = jnp.tile(cosine.reshape(-1, HD), (1, 2 * heads))
    sine = jnp.tile(sine.reshape(-1, HD), (1, 2 * heads))

    normed = normalize(patches)
    projected = jnp.dot(normed, fused, preferred_element_type=jnp.float32)
    width = heads * HD
    turned = projected[:, : 2 * width] * cosine + projected[:, 2 * width : 4 * width] * sine
    turned = turned.astype(jnp.bfloat16).reshape(windows, window_tokens, 2 * width)
    queries = turned[:, :, :width]
    key_block = turned[:, :, width:]
    values = projected[:, 4 * width :].astype(jnp.bfloat16).reshape(windows, window_tokens, width)

    lane_head = jnp.arange(width, dtype=jnp.int32) // HD
    scale = 1.0 / (HD ** 0.5)
    residual = patches.reshape(windows, QUARTERS, quarter_tokens, model_width)
    residual = lax.dynamic_index_in_dim(residual, mp_index, 1, keepdims=False)
    set_size = windows // WINDOW_SETS
    outputs = []
    for part in range(WINDOW_SETS):
        own = slice(part * set_size, (part + 1) * set_size)
        set_queries = queries[own]
        set_keys = key_block[own]
        set_values = values[own]
        mixed = jnp.zeros((set_size, window_tokens, width), jnp.float32)
        for head in range(heads):
            mask = lane_head == head
            picked = jnp.where(mask, set_queries, jnp.zeros_like(set_queries))
            scores = jnp.einsum(
                "wqd,wkd->wqk", picked, set_keys, preferred_element_type=jnp.float32
            ) * scale
            row_max = jnp.max(scores, axis=-1, keepdims=True)
            lifted = jnp.exp(scores - row_max)
            weights = (lifted / jnp.sum(lifted, axis=-1, keepdims=True)).astype(jnp.bfloat16)
            own_values = jnp.where(mask, set_values, jnp.zeros_like(set_values))
            mixed = mixed + jnp.einsum(
                "wqk,wkd->wqd", weights, own_values, preferred_element_type=jnp.float32
            )
        mixed = mixed.astype(jnp.bfloat16)

        spread = mixed.reshape(set_size, QUARTERS, quarter_tokens, 1, width)
        gathered = lax.all_to_all(spread, "mp", split_axis=1, concat_axis=3, tiled=True)
        gathered = gathered.reshape(set_size * quarter_tokens, QUARTERS * width)

        branch = lax.dot_general(
            gathered, out_full_t, (((1,), (1,)), ((), ())), preferred_element_type=jnp.float32
        )
        set_residual = residual[own].reshape(set_size * quarter_tokens, model_width)
        outputs.append((set_residual.astype(jnp.float32) + branch).astype(jnp.bfloat16))
    block_out = jnp.concatenate(outputs, axis=0)

    share_width = model_width // QUARTERS
    sectioned = block_out.reshape(page_count, quarter_tokens, QUARTERS, share_width)
    sectioned = jnp.transpose(sectioned, (0, 2, 1, 3)).reshape(
        page_count * QUARTERS, quarter_tokens, share_width
    )
    landed = lax.all_to_all(sectioned, ("seq", "mp"), split_axis=0, concat_axis=0, tiled=True)

    own_pages = page_count // seq_count
    first_page = seq_index * own_pages
    heights = lax.dynamic_slice_in_dim(page_rows, first_page, own_pages, 0)
    widths = lax.dynamic_slice_in_dim(page_cols, first_page, own_pages, 0)
    slot_rows = lax.dynamic_slice_in_dim(window_slot, first_page, own_pages, 0)
    block_count = slot_count * QUARTERS // own_pages

    landed = landed.reshape(own_pages, block_count, quarter_tokens, share_width)

    def regroup(received, height, page_width, slot_row):
        source, live = block_sources(height, page_width, slot_row, block_count)
        picked = jnp.take(received, source, axis=0)
        return jnp.where(live[:, None, None], picked, jnp.zeros_like(picked))

    merged = jax.vmap(regroup)(landed, heights, widths, slot_rows)
    return merged.reshape(-1, share_width)


def solution(mesh):
    return jax.shard_map(
        local,
        mesh=mesh,
        in_specs=(P("seq", None), P("seq", "mp"), P("mp", "seq"), P(), P(), P()),
        out_specs=P("seq", "mp"),
        check_vma=False,
    )
```

```python
import jax
import jax.numpy as jnp
from jax import lax
from jax.sharding import PartitionSpec as P

HD = 80
WS = 8
QUARTERS = 4


EPSILON = 1e-06


def angle_tables(row_place, column_place, head_size):
    quarter = head_size // 4
    frequency = 1.0 / 10000.0 ** (jnp.arange(quarter, dtype=jnp.float32) * 2.0 / (head_size // 2))
    angles = jnp.concatenate(
        [
            row_place[..., None].astype(jnp.float32) * frequency,
            column_place[..., None].astype(jnp.float32) * frequency,
        ],
        axis=-1,
    )
    angles = jnp.concatenate([angles, angles], axis=-1)
    return (jnp.cos(angles), jnp.sin(angles))


def slot_positions(page_widths, slot_table, slot_numbers, window_side):
    matches = slot_table[:, :, None] == slot_numbers[None, None, :]
    ordinal = jnp.arange(slot_table.shape[1], dtype=jnp.int32)
    window = jnp.sum(jnp.where(matches, ordinal[None, :, None], 0), axis=1)
    across = page_widths // window_side
    window_row = window // across[:, None]
    window_column = window % across[:, None]
    unit_side = window_side // 2
    position = jnp.arange(window_side * window_side, dtype=jnp.int32)
    merge_unit = position // 4
    corner = position % 4
    inner_row = merge_unit // unit_side * 2 + corner // 2
    inner_column = merge_unit % unit_side * 2 + corner % 2
    row_place = window_row[:, :, None] * window_side + inner_row
    column_place = window_column[:, :, None] * window_side + inner_column
    return (row_place, column_place)


def block_sources(height, page_width, slot_row, block_count):
    across = page_width // WS
    block = jnp.arange(block_count, dtype=jnp.int32)
    band = block // across
    column = block % across
    window_row = band // QUARTERS
    quarter = band % QUARTERS
    live = window_row < height // WS
    window = jnp.where(live, window_row * across + column, 0)
    ordinal = jnp.arange(slot_row.shape[0], dtype=jnp.int32)
    slot = jnp.sum(jnp.where(window[:, None] == ordinal[None, :], slot_row[None, :], 0), axis=1)
    return (slot * QUARTERS + quarter, live)


def normalize(block_in):
    values = block_in.astype(jnp.float32)
    factor = lax.rsqrt(jnp.mean(values * values, axis=-1, keepdims=True) + EPSILON)
    return (values * factor).astype(jnp.bfloat16)


def rotated_columns(weight):
    half = weight.shape[-1] // 2
    return jnp.concatenate([-weight[..., half:], weight[..., :half]], axis=-1)


def local(patches, w_qkv, w_out, page_rows, page_cols, window_slot):
    seq_index = lax.axis_index("seq")
    seq_count = lax.axis_size("seq")
    mp_index = lax.axis_index("mp")
    page_count = window_slot.shape[0]
    slot_count = window_slot.shape[1]
    slots_held = slot_count // seq_count
    window_tokens = WS * WS
    quarter_tokens = window_tokens // QUARTERS
    model_width = patches.shape[1]
    windows = patches.shape[0] // window_tokens

    own_rows = w_qkv.shape[0]
    heads = w_qkv.shape[1] // (3 * HD)
    qkv = w_qkv.reshape(own_rows, heads, 3, HD)
    w_q = qkv[:, :, 0]
    w_k = qkv[:, :, 1]
    fused_rows = jnp.concatenate(
        [
            w_q.reshape(own_rows, heads * HD),
            w_k.reshape(own_rows, heads * HD),
            rotated_columns(w_q).reshape(own_rows, heads * HD),
            rotated_columns(w_k).reshape(own_rows, heads * HD),
            qkv[:, :, 2].reshape(own_rows, heads * HD),
            w_out.T,
        ],
        axis=1,
    )
    joined = lax.all_gather(fused_rows, "seq", axis=0, tiled=True)
    fused = joined[:, : 5 * heads * HD]
    out_rows_t = joined[:, 5 * heads * HD :]
    out_full_t = lax.all_gather(out_rows_t, "mp", axis=1, tiled=True)

    slot_numbers = seq_index * slots_held + jnp.arange(slots_held, dtype=jnp.int32)
    row_place, column_place = slot_positions(page_cols, window_slot, slot_numbers, WS)
    cosine, sine = angle_tables(
        row_place.reshape(-1, window_tokens), column_place.reshape(-1, window_tokens), HD
    )
    cosine = jnp.tile(cosine.reshape(-1, HD), (1, 2 * heads))
    sine = jnp.tile(sine.reshape(-1, HD), (1, 2 * heads))

    normed = normalize(patches)
    projected = jnp.dot(normed, fused, preferred_element_type=jnp.float32)
    width = heads * HD
    turned = projected[:, : 2 * width] * cosine + projected[:, 2 * width : 4 * width] * sine
    turned = turned.astype(jnp.bfloat16).reshape(windows, window_tokens, 2 * width)
    queries = turned[:, :, :width]
    key_block = turned[:, :, width:]
    values = projected[:, 4 * width :].astype(jnp.bfloat16).reshape(windows, window_tokens, width)

    lane_head = jnp.arange(width, dtype=jnp.int32) // HD
    scale = 1.0 / (HD ** 0.5)
    mixed = jnp.zeros((windows, window_tokens, width), jnp.float32)
    for head in range(heads):
        mask = lane_head == head
        picked = jnp.where(mask, queries, jnp.zeros_like(queries))
        scores = jnp.einsum(
            "wqd,wkd->wqk", picked, key_block, preferred_element_type=jnp.float32
        ) * scale
        row_max = jnp.max(scores, axis=-1, keepdims=True)
        lifted = jnp.exp(scores - row_max)
        weights = (lifted / jnp.sum(lifted, axis=-1, keepdims=True)).astype(jnp.bfloat16)
        own_values = jnp.where(mask, values, jnp.zeros_like(values))
        mixed = mixed + jnp.einsum(
            "wqk,wkd->wqd", weights, own_values, preferred_element_type=jnp.float32
        )
    mixed = mixed.astype(jnp.bfloat16)

    spread = mixed.reshape(windows, QUARTERS, quarter_tokens, width)
    gathered = lax.all_to_all(spread, "mp", split_axis=1, concat_axis=1, tiled=True)
    out_grouped = out_full_t.reshape(model_width, QUARTERS, width)
    branch = lax.dot_general(
        gathered, out_grouped, (((1, 3), (1, 2)), ((), ())), preferred_element_type=jnp.float32
    )
    branch = branch.reshape(windows * quarter_tokens, model_width)
    residual = patches.reshape(windows, QUARTERS, quarter_tokens, model_width)
    residual = lax.dynamic_index_in_dim(residual, mp_index, 1, keepdims=False)
    residual = residual.reshape(windows * quarter_tokens, model_width).astype(jnp.float32)
    block_out = (residual + branch).astype(jnp.bfloat16)

    share_width = model_width // QUARTERS
    sectioned = block_out.reshape(page_count, quarter_tokens, QUARTERS, share_width)
    sectioned = jnp.transpose(sectioned, (0, 2, 1, 3)).reshape(
        page_count * QUARTERS, quarter_tokens, share_width
    )
    landed = lax.all_to_all(sectioned, ("seq", "mp"), split_axis=0, concat_axis=0, tiled=True)

    own_pages = page_count // seq_count
    first_page = seq_index * own_pages
    heights = lax.dynamic_slice_in_dim(page_rows, first_page, own_pages, 0)
    widths = lax.dynamic_slice_in_dim(page_cols, first_page, own_pages, 0)
    slot_rows = lax.dynamic_slice_in_dim(window_slot, first_page, own_pages, 0)
    block_count = slot_count * QUARTERS // own_pages

    landed = landed.reshape(own_pages, block_count, quarter_tokens, share_width)

    def regroup(received, height, page_width, slot_row):
        source, live = block_sources(height, page_width, slot_row, block_count)
        picked = jnp.take(received, source, axis=0)
        return jnp.where(live[:, None, None], picked, jnp.zeros_like(picked))

    merged = jax.vmap(regroup)(landed, heights, widths, slot_rows)
    return merged.reshape(-1, share_width)


def solution(mesh):
    return jax.shard_map(
        local,
        mesh=mesh,
        in_specs=(P("seq", None), P("seq", "mp"), P("mp", "seq"), P(), P(), P()),
        out_specs=P("seq", "mp"),
        check_vma=False,
    )
```
